256 devices in a mesh: det: 16 (over z, core), orb: 16 (over x, y).
Axes of the slice: x: 4, y: 4, z: 8, core: 2. Of those that a mesh axis runs over, the one named last changes fastest.
Arguments:
- orbitals: bfloat16 [64, 1024, 256], P('det', 'orb'), may hold values from -0.06 to 1.06
- dfit: bfloat16 [64, 1024, 1024], P('orb'), may hold values from -0.5 to 0.5, as said below
- pair_left: int32 [32], P('det'), may hold values from 0 to 63, as said below
- pair_right: int32 [32], P('det'), may hold values from 0 to 63
- pair_count: int32 [16], P('det'), may hold values from 1 to 2, as said below
- pair_weight: float32 [32], P('det'), may hold values from 1 to 4
- aux_screen: int32 [32, 64], P('det', 'orb'), may hold values 0 or 1
Outputs:
- gradient: float32 [64, 1024, 256], P('det', 'orb')
The draws below stay inside these ranges and needn't reach their ends.
Inputs may be any that keep to these rules, and one draw needn't show every extreme that they name: `pair_left`: slot s names a determinant among numbers (s // 2) * 4 to (s // 2 + 1) * 4 - 1. `pair_count`: some det index has all 2 slots live. `dfit`: every matrix is symmetric.
All inputs are finite; a program needn't handle non-finite values. No bound on the sum of `aux_screen` on one device may be relied on, other than what follows from the above.
Results may differ from the reference program's by a relative error of at most 0.0022.
Values may be sent and summed in bfloat16 or wider, within the bound.
No kernel may reach another device: no remote copies, remote signals or barrier semaphores. Data moves between devices by JAX's collectives and lax.ppermute only.
A program may use at most 64 MiB of HBM per device.

```python
import jax
import jax.numpy as jnp
from jax import lax

NBASIS = 1024
NOCC = 256
NAUX = 64
NS = 3
DET_DEV = 4
PAIR_CAP = 2
NDET = 64
NPAIRS = 32
N_DET = 16


def draw_orbitals(key, part):
    noise_key = jax.random.fold_in(key, 11)
    shape = (NDET, NBASIS, NOCC)
    noise = 0.01 * jax.random.truncated_normal(noise_key, -4.0, 4.0, shape, jnp.float32)
    basis = lax.broadcasted_iota(jnp.int32, (NBASIS, NOCC), 0)
    occupied = lax.broadcasted_iota(jnp.int32, (NBASIS, NOCC), 1)
    identity = (basis == occupied).astype(jnp.float32)
    return (identity[None, :, :] + noise).astype(jnp.bfloat16)


def draw_dfit(key, part):
    raw_key = jax.random.fold_in(key, 23)
    shape = (NAUX, NBASIS, NBASIS)
    raw = jax.random.truncated_normal(raw_key, -5.0, 5.0, shape, jnp.float32)
    factor = 0.7071 * NOCC ** (-0.5)
    symmetric = (raw + jnp.swapaxes(raw, 1, 2)) * factor
    return jnp.clip(symmetric, -0.5, 0.5).astype(jnp.bfloat16)


def draw_pair_left(key, part):
    total = N_DET * PAIR_CAP
    slots = jnp.arange(total, dtype=jnp.int32)
    offset = jax.random.randint(jax.random.fold_in(key, 31), (total,), 0, DET_DEV, jnp.int32)
    return slots // PAIR_CAP * DET_DEV + offset


def draw_pair_count(key, part):
    counts = jax.random.randint(jax.random.fold_in(key, 41), (N_DET,), 1, PAIR_CAP + 1, jnp.int32)
    filled = jax.random.randint(jax.random.fold_in(key, 43), (), 0, N_DET, jnp.int32)
    places = jnp.arange(N_DET, dtype=jnp.int32)
    return jnp.where(places == filled, PAIR_CAP, counts).astype(jnp.int32)


def plant(drawn, key, low, top_value):
    longest = drawn.shape.index(max(drawn.shape))
    spots = []
    for shift in (0, 1):
        where = [jax.random.randint(jax.random.fold_in(key, axis), (), 0, length) for axis, length in enumerate(drawn.shape)]
        where[longest] = (where[longest] + shift) % drawn.shape[longest]
        spots.append(tuple(where))
    return drawn.at[spots[0]].set(low).at[spots[1]].set(top_value)


def steps_of(key, shape, shards, least, largest):
    gain, own = 1.0, jax.random.fold_in(key, 6)
    for dim, blocks in shards:
        steps = jnp.exp(jax.random.uniform(jax.random.fold_in(own, dim), (blocks,), jnp.float32, least / len(shards), largest / len(shards)))
        gain = gain * jnp.repeat(steps, shape[dim] // blocks).reshape([-1 if axis == dim else 1 for axis in range(len(shape))])
    return gain


def setup_inputs(seed: int = 0) -> dict:
    key_list = jax.random.split(jax.random.key(seed), 8)
    orbitals = draw_orbitals(jax.random.fold_in(key_list[7], 71), 0)
    dfit = draw_dfit(jax.random.fold_in(key_list[7], 71), 0)
    pair_left = draw_pair_left(jax.random.fold_in(key_list[7], 71), 0)
    pair_right = plant(jax.random.randint(key_list[3], (NPAIRS,), 0, NDET), jax.random.fold_in(key_list[3], 1), 0, NDET - 1).astype(jnp.int32)
    pair_count = draw_pair_count(jax.random.fold_in(key_list[7], 71), 0)
    pair_weight = jnp.clip(1.0 + 3.0 * jax.random.uniform(key_list[5], (NPAIRS,), jnp.float32) ** steps_of(key_list[5], (NPAIRS,), ((0, 16),), -0.2, 0.2), 1.0, 4.0)
    aux_screen = plant((jax.random.randint(key_list[6], (NPAIRS, NAUX), 0, 4) < 3).astype(jnp.int32), jax.random.fold_in(key_list[6], 1), 0, 1)
    return {"orbitals": orbitals, "dfit": dfit, "pair_left": pair_left, "pair_right": pair_right, "pair_count": pair_count, "pair_weight": pair_weight, "aux_screen": aux_screen}


def newton(correlation):
    eye = jnp.eye(correlation.shape[-1], dtype=jnp.float32)
    inverse = eye
    for sweep in range(NS):
        product = jnp.dot(correlation, inverse, precision=lax.Precision.HIGHEST)
        inverse = jnp.dot(inverse, 2.0 * eye - product, precision=lax.Precision.HIGHEST)
    return inverse


def pair_terms(orbitals, dfit, left, right, weight, marks):
    left_orb = lax.dynamic_index_in_dim(orbitals, left, 0, keepdims=False)
    right_orb = lax.dynamic_index_in_dim(orbitals, right, 0, keepdims=False)
    correlation = jnp.dot(left_orb.T, right_orb, preferred_element_type=jnp.float32)
    inverse = newton(correlation)
    moved = jnp.dot(right_orb.astype(jnp.float32), inverse, precision=lax.Precision.HIGHEST).astype(jnp.bfloat16)

    def per_block(carry, inputs):
        block, mark_one = inputs
        applied = jnp.dot(block, moved, preferred_element_type=jnp.float32).astype(jnp.bfloat16)
        projected = jnp.dot(left_orb.T, block, preferred_element_type=jnp.float32).astype(jnp.bfloat16)
        exchange = jnp.dot(projected, moved, preferred_element_type=jnp.float32)
        scaled = (2.0 * weight * mark_one * exchange).astype(jnp.bfloat16)
        left_acc = carry[0] + jnp.dot(applied, scaled.T, preferred_element_type=jnp.float32)
        moved_acc = carry[1] + jnp.dot(projected.T, scaled, preferred_element_type=jnp.float32)
        return (left_acc, moved_acc), None

    zeros = jnp.zeros((NBASIS, NOCC), jnp.float32)
    (left_grad, moved_grad), unused = lax.scan(per_block, (zeros, zeros), (dfit, marks))
    right_grad = jnp.dot(moved_grad, inverse.T, precision=lax.Precision.HIGHEST)
    return left_grad, right_grad


def reference(orbitals, dfit, pair_left, pair_right, pair_count, pair_weight, aux_screen):
    total = pair_left.shape[0]
    capacity = total // pair_count.shape[0]
    slots = jnp.arange(total, dtype=jnp.int32)
    live = (slots % capacity) < pair_count[slots // capacity]
    weights = jnp.where(live, pair_weight, jnp.zeros_like(pair_weight)).astype(jnp.float32)
    marks = aux_screen.astype(jnp.float32)
    zeros = jnp.zeros((NBASIS, NOCC), jnp.float32)

    def visit(grad, inputs):
        left, right, weight, mark_row = inputs
        left_grad, right_grad = lax.cond(
            weight != 0.0,
            lambda: pair_terms(orbitals, dfit, left, right, weight, mark_row),
            lambda: (zeros, zeros))
        grad = grad.at[left].add(left_grad)
        grad = grad.at[right].add(right_grad)
        return grad, None

    start_grad = jnp.zeros((NDET, NBASIS, NOCC), jnp.float32)
    grad, unused = lax.scan(visit, start_grad, (pair_left, pair_right, weights, marks))
    return grad
```

```python
import jax
import jax.numpy as jnp
from jax import lax
from jax.sharding import PartitionSpec as P

NS = 3
HI = lax.Precision.HIGHEST


def newton(correlation):
    eye = jnp.eye(correlation.shape[-1], dtype=jnp.float32)
    inverse = 2.0 * eye - correlation
    for sweep in range(NS - 1):
        product = jnp.einsum("bij,bjk->bik", correlation, inverse, precision=HI)
        inverse = jnp.einsum("bij,bjk->bik", inverse, 2.0 * eye - product, precision=HI)
    return inverse


def local(orbitals, dfit, pair_left, pair_right, pair_count, pair_weight, aux_screen):
    det_local, rows, nocc = orbitals.shape
    capacity = pair_left.shape[0]
    n_det = lax.axis_size("det")
    n_orb = lax.axis_size("orb")
    me = lax.axis_index("det")
    slot_index = jnp.arange(capacity, dtype=jnp.int32)
    weights = jnp.where(slot_index < pair_count[0], pair_weight, jnp.zeros_like(pair_weight))
    left_local = pair_left % det_local
    left_rows = jnp.take(orbitals, left_local, axis=0)

    right_all = lax.all_gather(pair_right, "det", axis=0, tiled=True)
    send = jnp.take(orbitals, right_all % det_local, axis=0).reshape(n_det, capacity, rows, nocc)
    got = lax.all_to_all(send, "det", 0, 0, tiled=True)
    owner = pair_right // det_local
    right_rows = got[owner, slot_index]

    both = jnp.concatenate([left_rows, right_rows], axis=0)
    spread = jnp.broadcast_to(both[None], (n_orb,) + both.shape)
    gathered = lax.all_to_all(spread, "orb", 0, 0, tiled=True)
    gathered = jnp.transpose(gathered, (1, 0, 2, 3)).reshape(2 * capacity, n_orb * rows, nocc)
    left_full = gathered[:capacity]
    right_full = gathered[capacity:]

    correlation = jnp.einsum("brc,brd->bcd", left_full, right_full, preferred_element_type=jnp.float32)
    inverse = newton(correlation)
    moved_full = jnp.einsum(
        "brc,bcd->brd", right_full.astype(jnp.float32), inverse, precision=HI
    ).astype(jnp.bfloat16)

    stacked = jnp.concatenate([moved_full, left_full], axis=2)
    stacked = jnp.transpose(stacked, (1, 0, 2)).reshape(n_orb * rows, capacity * 2 * nocc)
    product = jnp.einsum("qst,tk->qsk", dfit, stacked, preferred_element_type=jnp.float32).astype(jnp.bfloat16)
    product = product.reshape(dfit.shape[0], n_orb * rows, capacity, 2, nocc)
    applied = product[:, :, :, 0]
    projected_t = product[:, :, :, 1]
    exchange = jnp.einsum("qtbc,btd->bqcd", projected_t, moved_full, preferred_element_type=jnp.float32)
    factor = 2.0 * weights[:, None, None, None] * aux_screen.astype(jnp.float32)[:, :, None, None]
    scaled = (factor * exchange).astype(jnp.bfloat16)
    left_term = jnp.einsum("qsbc,bqdc->bsd", applied, scaled, preferred_element_type=jnp.float32)
    moved_term = jnp.einsum("qsbc,bqcd->bsd", projected_t, scaled, preferred_element_type=jnp.float32)

    terms = jnp.stack([left_term, moved_term], axis=0).reshape(2, capacity, n_orb, rows, nocc)
    terms = jnp.transpose(terms, (2, 0, 1, 3, 4))
    parts = lax.all_to_all(terms, "orb", 0, 0, tiled=True)
    summed = jnp.sum(parts, axis=0)
    left_grad = summed[0]
    moved_grad = summed[1]
    right_grad = jnp.einsum("brc,bdc->brd", moved_grad, inverse, precision=HI)

    own = left_local[:, None] == jnp.arange(det_local, dtype=jnp.int32)[None, :]
    own_sum = jnp.sum(jnp.where(own[:, :, None, None], left_grad[:, None], 0.0), axis=0)

    back = jnp.broadcast_to(right_grad[None], (n_det,) + right_grad.shape)
    came = lax.all_to_all(back, "det", 0, 0, tiled=True)
    mine = right_all.reshape(n_det, capacity)[:, :, None] == (
        me * det_local + jnp.arange(det_local, dtype=jnp.int32)
    )[None, None, :]
    returned = jnp.sum(jnp.where(mine[:, :, :, None, None], came[:, :, None], 0.0), axis=(0, 1))
    return own_sum + returned


def solution(mesh):
    in_specs = (
        P("det", "orb", None),
        P("orb", None, None),
        P("det"),
        P("det"),
        P("det"),
        P("det"),
        P("det", "orb"),
    )
    out_specs = P("det", "orb", None)
    return jax.shard_map(local, mesh=mesh, in_specs=in_specs, out_specs=out_specs, check_vma=False)
```

```python
import jax
import jax.numpy as jnp
from jax import lax
from jax.sharding import PartitionSpec as P

NS = 3
HI = lax.Precision.HIGHEST


def newton(correlation):
    eye = jnp.eye(correlation.shape[-1], dtype=jnp.float32)
    inverse = 2.0 * eye - correlation
    for sweep in range(NS - 1):
        product = jnp.einsum("bij,bjk->bik", correlation, inverse, precision=HI)
        inverse = jnp.einsum("bij,bjk->bik", inverse, 2.0 * eye - product, precision=HI)
    return inverse


def gather_rows(rows_local, n_orb):
    spread = jnp.broadcast_to(rows_local[None], (n_orb,) + rows_local.shape)
    got = lax.all_to_all(spread, "orb", 0, 0, tiled=True)
    count, rows, nocc = rows_local.shape
    return jnp.transpose(got, (1, 0, 2, 3)).reshape(count, n_orb * rows, nocc)


def scatter_rows(full, n_orb):
    count, total, nocc = full.shape
    parts = jnp.transpose(full.reshape(count, n_orb, total // n_orb, nocc), (1, 0, 2, 3))
    got = lax.all_to_all(parts, "orb", 0, 0, tiled=True)
    return jnp.sum(got, axis=0)


def local(orbitals, dfit, pair_left, pair_right, pair_count, pair_weight, aux_screen):
    det_local, rows, nocc = orbitals.shape
    capacity = pair_left.shape[0]
    n_det = lax.axis_size("det")
    n_orb = lax.axis_size("orb")
    me = lax.axis_index("det")
    slot_index = jnp.arange(capacity, dtype=jnp.int32)
    weights = jnp.where(slot_index < pair_count[0], pair_weight, jnp.zeros_like(pair_weight))
    left_local = pair_left % det_local
    left_rows = jnp.take(orbitals, left_local, axis=0)
    left_full = gather_rows(left_rows, n_orb)

    right_all = lax.all_to_all(
        jnp.broadcast_to(pair_right[None], (n_det, capacity)), "det", 0, 0, tiled=True
    ).reshape(n_det * capacity)
    send = jnp.take(orbitals, right_all % det_local, axis=0).reshape(n_det, capacity, rows, nocc)
    got = lax.all_to_all(send, "det", 0, 0, tiled=True)
    owner = pair_right // det_local
    right_rows = got[owner, slot_index]
    right_full = gather_rows(right_rows, n_orb)

    left_stack = jnp.transpose(left_full, (1, 0, 2)).reshape(n_orb * rows, capacity * nocc)
    projected_t = jnp.einsum(
        "qst,tk->qsk", dfit, left_stack, preferred_element_type=jnp.float32
    ).astype(jnp.bfloat16).reshape(dfit.shape[0], n_orb * rows, capacity, nocc)

    correlation = jnp.einsum("brc,brd->bcd", left_full, right_full, preferred_element_type=jnp.float32)
    inverse = newton(correlation)
    moved_full = jnp.einsum(
        "brc,bcd->brd", right_full.astype(jnp.float32), inverse, precision=HI
    ).astype(jnp.bfloat16)
    moved_stack = jnp.transpose(moved_full, (1, 0, 2)).reshape(n_orb * rows, capacity * nocc)
    applied = jnp.einsum(
        "qst,tk->qsk", dfit, moved_stack, preferred_element_type=jnp.float32
    ).astype(jnp.bfloat16).reshape(dfit.shape[0], n_orb * rows, capacity, nocc)

    exchange = jnp.einsum("qtbc,btd->bqcd", projected_t, moved_full, preferred_element_type=jnp.float32)
    factor = 2.0 * weights[:, None, None, None] * aux_screen.astype(jnp.float32)[:, :, None, None]
    scaled = (factor * exchange).astype(jnp.bfloat16)
    moved_term = jnp.einsum("qsbc,bqcd->bsd", projected_t, scaled, preferred_element_type=jnp.float32)
    moved_grad = scatter_rows(moved_term, n_orb)
    right_grad = jnp.einsum("brc,bdc->brd", moved_grad, inverse, precision=HI)

    back = jnp.broadcast_to(right_grad[None], (n_det,) + right_grad.shape)
    came = lax.all_to_all(back, "det", 0, 0, tiled=True)

    left_term = jnp.einsum("qsbc,bqdc->bsd", applied, scaled, preferred_element_type=jnp.float32)
    left_grad = scatter_rows(left_term, n_orb)
    own = left_local[:, None] == jnp.arange(det_local, dtype=jnp.int32)[None, :]
    own_sum = jnp.sum(jnp.where(own[:, :, None, None], left_grad[:, None], 0.0), axis=0)

    mine = right_all.reshape(n_det, capacity)[:, :, None] == (
        me * det_local + jnp.arange(det_local, dtype=jnp.int32)
    )[None, None, :]
    returned = jnp.sum(jnp.where(mine[:, :, :, None, None], came[:, :, None], 0.0), axis=(0, 1))
    return own_sum + returned


def solution(mesh):
    in_specs = (
        P("det", "orb", None),
        P("orb", None, None),
        P("det"),
        P("det"),
        P("det"),
        P("det"),
        P("det", "orb"),
    )
    out_specs = P("det", "orb", None)
    return jax.shard_map(local, mesh=mesh, in_specs=in_specs, out_specs=out_specs, check_vma=False)
```

```python
import jax
import jax.numpy as jnp
from jax import lax
from jax.sharding import PartitionSpec as P

NS = 3
HI = lax.Precision.HIGHEST


def newton(correlation):
    eye = jnp.eye(correlation.shape[-1], dtype=jnp.float32)
    inverse = 2.0 * eye - correlation
    for sweep in range(NS - 1):
        product = jnp.einsum("bij,bjk->bik", correlation, inverse, precision=HI)
        inverse = jnp.einsum("bij,bjk->bik", inverse, 2.0 * eye - product, precision=HI)
    return inverse


def gather_rows(rows_local, n_orb):
    spread = jnp.broadcast_to(rows_local[None], (n_orb,) + rows_local.shape)
    got = lax.all_to_all(spread, "orb", 0, 0, tiled=True)
    count, rows, nocc = rows_local.shape
    return jnp.transpose(got, (1, 0, 2, 3)).reshape(count, n_orb * rows, nocc)


def scatter_rows(full, n_orb):
    count, total, nocc = full.shape
    parts = jnp.transpose(full.reshape(count, n_orb, total // n_orb, nocc), (1, 0, 2, 3))
    got = lax.all_to_all(parts, "orb", 0, 0, tiled=True)
    return jnp.sum(got, axis=0)


def det_shifts(send_to, n_det):
    got = [send_to(0)]
    for shift in range(1, n_det):
        pairs = [(i, (i + shift) % n_det) for i in range(n_det)]
        got.append(lax.ppermute(send_to(shift), "det", pairs))
    return jnp.stack(got)


def local(orbitals, dfit, pair_left, pair_right, pair_count, pair_weight, aux_screen):
    det_local, rows, nocc = orbitals.shape
    capacity = pair_left.shape[0]
    n_det = lax.axis_size("det")
    n_orb = lax.axis_size("orb")
    me = lax.axis_index("det")
    slot_index = jnp.arange(capacity, dtype=jnp.int32)
    weights = jnp.where(slot_index < pair_count[0], pair_weight, jnp.zeros_like(pair_weight))
    left_local = pair_left % det_local
    left_rows = jnp.take(orbitals, left_local, axis=0)

    right_all = lax.all_gather(pair_right.astype(jnp.float32), "det", axis=0, tiled=True).astype(jnp.int32)
    left_full = gather_rows(left_rows, n_orb)

    send = jnp.take(orbitals, right_all % det_local, axis=0).reshape(n_det, capacity, rows, nocc)
    got = det_shifts(lambda k: send[(me + k) % n_det], n_det)
    owner = pair_right // det_local
    right_rows = got[(me - owner) % n_det, slot_index]
    right_full = gather_rows(right_rows, n_orb)

    left_stack = jnp.transpose(left_full, (1, 0, 2)).reshape(n_orb * rows, capacity * nocc)
    projected_t = jnp.einsum(
        "qst,tk->qsk", dfit, left_stack, preferred_element_type=jnp.float32
    ).astype(jnp.bfloat16).reshape(dfit.shape[0], n_orb * rows, capacity, nocc)

    correlation = jnp.einsum("brc,brd->bcd", left_full, right_full, preferred_element_type=jnp.float32)
    inverse = newton(correlation)
    moved_full = jnp.einsum(
        "brc,bcd->brd", right_full.astype(jnp.float32), inverse, precision=HI
    ).astype(jnp.bfloat16)
    moved_stack = jnp.transpose(moved_full, (1, 0, 2)).reshape(n_orb * rows, capacity * nocc)
    applied = jnp.einsum(
        "qst,tk->qsk", dfit, moved_stack, preferred_element_type=jnp.float32
    ).astype(jnp.bfloat16).reshape(dfit.shape[0], n_orb * rows, capacity, nocc)

    exchange = jnp.einsum("qtbc,btd->bqcd", projected_t, moved_full, preferred_element_type=jnp.float32)
    factor = 2.0 * weights[:, None, None, None] * aux_screen.astype(jnp.float32)[:, :, None, None]
    scaled = (factor * exchange).astype(jnp.bfloat16)
    moved_term = jnp.einsum("qsbc,bqcd->bsd", projected_t, scaled, preferred_element_type=jnp.float32)
    moved_grad = scatter_rows(moved_term, n_orb)
    right_grad = jnp.einsum("brc,bdc->brd", moved_grad, inverse, precision=HI)

    came = det_shifts(lambda k: right_grad, n_det)

    left_term = jnp.einsum("qsbc,bqdc->bsd", applied, scaled, preferred_element_type=jnp.float32)
    left_grad = scatter_rows(left_term, n_orb)
    own = left_local[:, None] == jnp.arange(det_local, dtype=jnp.int32)[None, :]
    own_sum = jnp.sum(jnp.where(own[:, :, None, None], left_grad[:, None], 0.0), axis=0)

    source = (me - jnp.arange(n_det, dtype=jnp.int32)) % n_det
    asked = right_all.reshape(n_det, capacity)[source]
    mine = asked[:, :, None] == (me * det_local + jnp.arange(det_local, dtype=jnp.int32))[None, None, :]
    returned = jnp.sum(jnp.where(mine[:, :, :, None, None], came[:, :, None], 0.0), axis=(0, 1))
    return own_sum + returned


def solution(mesh):
    in_specs = (
        P("det", "orb", None),
        P("orb", None, None),
        P("det"),
        P("det"),
        P("det"),
        P("det"),
        P("det", "orb"),
    )
    out_specs = P("det", "orb", None)
    return jax.shard_map(local, mesh=mesh, in_specs=in_specs, out_specs=out_specs, check_vma=False)
```

```python
import jax
import jax.numpy as jnp
from jax import lax
from jax.sharding import PartitionSpec as P

NS = 3
HI = lax.Precision.HIGHEST


def newton(correlation):
    eye = jnp.eye(correlation.shape[-1], dtype=jnp.float32)
    inverse = 2.0 * eye - correlation
    for sweep in range(NS - 1):
        product = jnp.einsum("bij,bjk->bik", correlation, inverse, precision=HI)
        inverse = jnp.einsum("bij,bjk->bik", inverse, 2.0 * eye - product, precision=HI)
    return inverse


def gather_rows(rows_local, n_orb):
    spread = jnp.broadcast_to(rows_local[None], (n_orb,) + rows_local.shape)
    got = lax.all_to_all(spread, "orb", 0, 0, tiled=True)
    count, rows, nocc = rows_local.shape
    return jnp.transpose(got, (1, 0, 2, 3)).reshape(count, n_orb * rows, nocc)


def scatter_rows(full, n_orb):
    count, total, nocc = full.shape
    parts = jnp.transpose(full.reshape(count, n_orb, total // n_orb, nocc), (1, 0, 2, 3))
    got = lax.all_to_all(parts, "orb", 0, 0, tiled=True)
    return jnp.sum(got, axis=0)


def local(orbitals, dfit, pair_left, pair_right, pair_count, pair_weight, aux_screen):
    det_local, rows, nocc = orbitals.shape
    capacity = pair_left.shape[0]
    n_det = lax.axis_size("det")
    n_orb = lax.axis_size("orb")
    me = lax.axis_index("det")
    slot_index = jnp.arange(capacity, dtype=jnp.int32)
    weights = jnp.where(slot_index < pair_count[0], pair_weight, jnp.zeros_like(pair_weight))
    left_local = pair_left % det_local
    left_rows = jnp.take(orbitals, left_local, axis=0)

    marks = jnp.zeros((1, rows * nocc), jnp.bfloat16).at[0, :capacity].set(pair_right.astype(jnp.bfloat16))
    carried = jnp.concatenate([orbitals, marks.reshape(1, rows, nocc)], axis=0)
    everyone = lax.all_gather(carried, "det", axis=0, tiled=False)
    right_all = everyone[:, det_local].reshape(n_det, rows * nocc)[:, :capacity].astype(jnp.int32).reshape(-1)
    left_full = gather_rows(left_rows, n_orb)
    right_rows = everyone[pair_right // det_local, pair_right % det_local]
    right_full = gather_rows(right_rows, n_orb)

    left_stack = jnp.transpose(left_full, (1, 0, 2)).reshape(n_orb * rows, capacity * nocc)
    projected_t = jnp.einsum(
        "qst,tk->qsk", dfit, left_stack, preferred_element_type=jnp.float32
    ).astype(jnp.bfloat16).reshape(dfit.shape[0], n_orb * rows, capacity, nocc)

    correlation = jnp.einsum("brc,brd->bcd", left_full, right_full, preferred_element_type=jnp.float32)
    inverse = newton(correlation)
    moved_full = jnp.einsum(
        "brc,bcd->brd", right_full.astype(jnp.float32), inverse, precision=HI
    ).astype(jnp.bfloat16)
    moved_stack = jnp.transpose(moved_full, (1, 0, 2)).reshape(n_orb * rows, capacity * nocc)
    applied = jnp.einsum(
        "qst,tk->qsk", dfit, moved_stack, preferred_element_type=jnp.float32
    ).astype(jnp.bfloat16).reshape(dfit.shape[0], n_orb * rows, capacity, nocc)

    exchange = jnp.einsum("qtbc,btd->bqcd", projected_t, moved_full, preferred_element_type=jnp.float32)
    factor = 2.0 * weights[:, None, None, None] * aux_screen.astype(jnp.float32)[:, :, None, None]
    scaled = (factor * exchange).astype(jnp.bfloat16)
    moved_term = jnp.einsum("qsbc,bqcd->bsd", projected_t, scaled, preferred_element_type=jnp.float32)
    moved_grad = scatter_rows(moved_term, n_orb)
    right_grad = jnp.einsum("brc,bdc->brd", moved_grad, inverse, precision=HI)

    came = lax.all_gather(right_grad, "det", axis=0, tiled=False)

    left_term = jnp.einsum("qsbc,bqdc->bsd", applied, scaled, preferred_element_type=jnp.float32)
    left_grad = scatter_rows(left_term, n_orb)
    own = left_local[:, None] == jnp.arange(det_local, dtype=jnp.int32)[None, :]
    own_sum = jnp.sum(jnp.where(own[:, :, None, None], left_grad[:, None], 0.0), axis=0)

    asked = right_all.reshape(n_det, capacity)
    mine = asked[:, :, None] == (me * det_local + jnp.arange(det_local, dtype=jnp.int32))[None, None, :]
    returned = jnp.sum(jnp.where(mine[:, :, :, None, None], came[:, :, None], 0.0), axis=(0, 1))
    return own_sum + returned


def solution(mesh):
    in_specs = (
        P("det", "orb", None),
        P("orb", None, None),
        P("det"),
        P("det"),
        P("det"),
        P("det"),
        P("det", "orb"),
    )
    out_specs = P("det", "orb", None)
    return jax.shard_map(local, mesh=mesh, in_specs=in_specs, out_specs=out_specs, check_vma=False)
```

```python
import jax
import jax.numpy as jnp
from jax import lax
from jax.sharding import PartitionSpec as P

NS = 3
HI = lax.Precision.HIGHEST


def newton(correlation):
    eye = jnp.eye(correlation.shape[-1], dtype=jnp.float32)
    inverse = 2.0 * eye - correlation
    for sweep in range(NS - 1):
        product = jnp.einsum("bij,bjk->bik", correlation, inverse, precision=HI)
        inverse = jnp.einsum("bij,bjk->bik", inverse, 2.0 * eye - product, precision=HI)
    return inverse


def gather_rows(rows_local, n_orb):
    spread = jnp.broadcast_to(rows_local[None], (n_orb,) + rows_local.shape)
    got = lax.all_to_all(spread, "orb", 0, 0, tiled=True)
    count, rows, nocc = rows_local.shape
    return jnp.transpose(got, (1, 0, 2, 3)).reshape(count, n_orb * rows, nocc)


def scatter_rows(full, n_orb):
    count, total, nocc = full.shape
    parts = jnp.transpose(full.reshape(count, n_orb, total // n_orb, nocc), (1, 0, 2, 3))
    got = lax.all_to_all(parts, "orb", 0, 0, tiled=True)
    return jnp.sum(got, axis=0)


def local(orbitals, dfit, pair_left, pair_right, pair_count, pair_weight, aux_screen):
    det_local, rows, nocc = orbitals.shape
    capacity = pair_left.shape[0]
    n_det = lax.axis_size("det")
    n_orb = lax.axis_size("orb")
    me = lax.axis_index("det")
    slot_index = jnp.arange(capacity, dtype=jnp.int32)
    weights = jnp.where(slot_index < pair_count[0], pair_weight, jnp.zeros_like(pair_weight))
    left_local = pair_left % det_local
    left_rows = jnp.take(orbitals, left_local, axis=0)

    pad = 16
    marks = jnp.zeros((pad, nocc), jnp.bfloat16).at[0, :capacity].set(pair_right.astype(jnp.bfloat16))
    carried = jnp.concatenate([orbitals.reshape(det_local * rows, nocc), marks], axis=0)
    everyone = lax.all_gather(carried, "det", axis=0, tiled=False)
    right_all = everyone[:, det_local * rows, :capacity].astype(jnp.int32).reshape(-1)
    fetched = everyone[:, : det_local * rows].reshape(n_det * det_local, rows, nocc)
    left_full = gather_rows(left_rows, n_orb)
    right_rows = fetched[pair_right]
    right_full = gather_rows(right_rows, n_orb)

    left_stack = jnp.transpose(left_full, (1, 0, 2)).reshape(n_orb * rows, capacity * nocc)
    projected_t = jnp.einsum(
        "qst,tk->qsk", dfit, left_stack, preferred_element_type=jnp.float32
    ).astype(jnp.bfloat16).reshape(dfit.shape[0], n_orb * rows, capacity, nocc)

    correlation = jnp.einsum("brc,brd->bcd", left_full, right_full, preferred_element_type=jnp.float32)
    inverse = newton(correlation)
    moved_full = jnp.einsum(
        "brc,bcd->brd", right_full.astype(jnp.float32), inverse, precision=HI
    ).astype(jnp.bfloat16)
    moved_stack = jnp.transpose(moved_full, (1, 0, 2)).reshape(n_orb * rows, capacity * nocc)
    applied = jnp.einsum(
        "qst,tk->qsk", dfit, moved_stack, preferred_element_type=jnp.float32
    ).astype(jnp.bfloat16).reshape(dfit.shape[0], n_orb * rows, capacity, nocc)

    exchange = jnp.einsum("qtbc,btd->bqcd", projected_t, moved_full, preferred_element_type=jnp.float32)
    factor = 2.0 * weights[:, None, None, None] * aux_screen.astype(jnp.float32)[:, :, None, None]
    scaled = (factor * exchange).astype(jnp.bfloat16)
    moved_term = jnp.einsum("qsbc,bqcd->bsd", projected_t, scaled, preferred_element_type=jnp.float32)
    moved_grad = scatter_rows(moved_term, n_orb)
    right_grad = jnp.einsum("brc,bdc->brd", moved_grad, inverse, precision=HI)

    came = lax.all_gather(right_grad, "det", axis=0, tiled=False)

    left_term = jnp.einsum("qsbc,bqdc->bsd", applied, scaled, preferred_element_type=jnp.float32)
    left_grad = scatter_rows(left_term, n_orb)
    own = left_local[:, None] == jnp.arange(det_local, dtype=jnp.int32)[None, :]
    own_sum = jnp.sum(jnp.where(own[:, :, None, None], left_grad[:, None], 0.0), axis=0)

    asked = right_all.reshape(n_det, capacity)
    mine = asked[:, :, None] == (me * det_local + jnp.arange(det_local, dtype=jnp.int32))[None, None, :]
    returned = jnp.sum(jnp.where(mine[:, :, :, None, None], came[:, :, None], 0.0), axis=(0, 1))
    return own_sum + returned


def solution(mesh):
    in_specs = (
        P("det", "orb", None),
        P("orb", None, None),
        P("det"),
        P("det"),
        P("det"),
        P("det"),
        P("det", "orb"),
    )
    out_specs = P("det", "orb", None)
    return jax.shard_map(local, mesh=mesh, in_specs=in_specs, out_specs=out_specs, check_vma=False)
```

```python
import jax
import jax.numpy as jnp
from jax import lax
from jax.sharding import PartitionSpec as P

NS = 3
HI = lax.Precision.HIGHEST


def newton(correlation):
    eye = jnp.eye(correlation.shape[-1], dtype=jnp.float32)
    inverse = 2.0 * eye - correlation
    for sweep in range(NS - 1):
        product = jnp.einsum("bij,bjk->bik", correlation, inverse, precision=HI)
        inverse = jnp.einsum("bij,bjk->bik", inverse, 2.0 * eye - product, precision=HI)
    return inverse


def gather_rows(rows_local, n_orb):
    spread = jnp.broadcast_to(rows_local[None], (n_orb,) + rows_local.shape)
    got = lax.all_to_all(spread, "orb", 0, 0, tiled=True)
    count, rows, nocc = rows_local.shape
    return jnp.transpose(got, (1, 0, 2, 3)).reshape(count, n_orb * rows, nocc)


def scatter_rows(full, n_orb):
    count, total, nocc = full.shape
    parts = jnp.transpose(full.reshape(count, n_orb, total // n_orb, nocc), (1, 0, 2, 3))
    got = lax.all_to_all(parts, "orb", 0, 0, tiled=True)
    return jnp.sum(got, axis=0)


def local(orbitals, dfit, pair_left, pair_right, pair_count, pair_weight, aux_screen):
    det_local, rows, nocc = orbitals.shape
    capacity = pair_left.shape[0]
    n_det = lax.axis_size("det")
    n_orb = lax.axis_size("orb")
    me = lax.axis_index("det")
    slot_index = jnp.arange(capacity, dtype=jnp.int32)
    weights = jnp.where(slot_index < pair_count[0], pair_weight, jnp.zeros_like(pair_weight))
    left_local = pair_left % det_local
    left_rows = jnp.take(orbitals, left_local, axis=0)

    pad = 16
    marks = jnp.zeros((pad, nocc), jnp.bfloat16).at[0, :capacity].set(pair_right.astype(jnp.bfloat16))
    carried = jnp.concatenate([orbitals.reshape(det_local * rows, nocc), marks], axis=0)
    everyone = lax.all_gather(carried, "det", axis=0, tiled=False)
    right_all = everyone[:, det_local * rows, :capacity].astype(jnp.int32).reshape(-1)
    fetched = everyone[:, : det_local * rows].reshape(n_det * det_local, rows, nocc)
    left_full = gather_rows(left_rows, n_orb)
    right_rows = fetched[pair_right]
    right_full = gather_rows(right_rows, n_orb)

    left_stack = jnp.transpose(left_full, (1, 0, 2)).reshape(n_orb * rows, capacity * nocc)
    projected_t = jnp.einsum(
        "qst,tk->qsk", dfit, left_stack, preferred_element_type=jnp.float32
    ).astype(jnp.bfloat16).reshape(dfit.shape[0], n_orb * rows, capacity, nocc)

    correlation = jnp.einsum("brc,brd->bcd", left_full, right_full, preferred_element_type=jnp.float32)
    inverse = newton(correlation)
    moved_full = jnp.einsum(
        "brc,bcd->brd", right_full.astype(jnp.float32), inverse, precision=HI
    ).astype(jnp.bfloat16)
    moved_stack = jnp.transpose(moved_full, (1, 0, 2)).reshape(n_orb * rows, capacity * nocc)
    applied = jnp.einsum(
        "qst,tk->qsk", dfit, moved_stack, preferred_element_type=jnp.float32
    ).astype(jnp.bfloat16).reshape(dfit.shape[0], n_orb * rows, capacity, nocc)

    exchange = jnp.einsum("qtbc,btd->bqcd", projected_t, moved_full, preferred_element_type=jnp.float32)
    factor = 2.0 * weights[:, None, None, None] * aux_screen.astype(jnp.float32)[:, :, None, None]
    scaled = (factor * exchange).astype(jnp.bfloat16)
    moved_term = jnp.einsum("qsbc,bqcd->bsd", projected_t, scaled, preferred_element_type=jnp.float32)
    moved_grad = scatter_rows(moved_term, n_orb)
    live = (weights != 0.0)[:, None, None]
    right_grad = jnp.where(live, jnp.einsum("brc,bdc->brd", moved_grad, inverse, precision=HI), 0.0)

    came = lax.all_gather(right_grad, "det", axis=0, tiled=False)

    left_term = jnp.einsum("qsbc,bqdc->bsd", applied, scaled, preferred_element_type=jnp.float32)
    left_grad = jnp.where(live, scatter_rows(left_term, n_orb), 0.0)
    own = left_local[:, None] == jnp.arange(det_local, dtype=jnp.int32)[None, :]
    own_sum = jnp.sum(jnp.where(own[:, :, None, None], left_grad[:, None], 0.0), axis=0)

    asked = right_all.reshape(n_det, capacity)
    mine = asked[:, :, None] == (me * det_local + jnp.arange(det_local, dtype=jnp.int32))[None, None, :]
    returned = jnp.sum(jnp.where(mine[:, :, :, None, None], came[:, :, None], 0.0), axis=(0, 1))
    return own_sum + returned


def solution(mesh):
    in_specs = (
        P("det", "orb", None),
        P("orb", None, None),
        P("det"),
        P("det"),
        P("det"),
        P("det"),
        P("det", "orb"),
    )
    out_specs = P("det", "orb", None)
    return jax.shard_map(local, mesh=mesh, in_specs=in_specs, out_specs=out_specs, check_vma=False)
```

```python
import jax
import jax.numpy as jnp
from jax import lax
from jax.sharding import PartitionSpec as P

NS = 3
HI = lax.Precision.HIGHEST


def newton(correlation):
    eye = jnp.eye(correlation.shape[-1], dtype=jnp.float32)
    inverse = 2.0 * eye - correlation
    for _ in range(NS - 1):
        product = jnp.einsum("bij,bjk->bik", correlation, inverse, precision=HI)
        inverse = jnp.einsum("bij,bjk->bik", inverse, 2.0 * eye - product, precision=HI)
    return inverse


def gather_rows(rows_local, n_orb):
    spread = jnp.broadcast_to(rows_local[None], (n_orb,) + rows_local.shape)
    got = lax.all_to_all(spread, "orb", 0, 0, tiled=True)
    count, rows, nocc = rows_local.shape
    return jnp.transpose(got, (1, 0, 2, 3)).reshape(count, n_orb * rows, nocc)


def scatter_rows(full, n_orb):
    count, total, nocc = full.shape
    parts = jnp.transpose(full.reshape(count, n_orb, total // n_orb, nocc), (1, 0, 2, 3))
    got = lax.all_to_all(parts, "orb", 0, 0, tiled=True)
    return jnp.sum(got, axis=0)


def local_body(orbitals, dfit, pair_left, pair_right, pair_count, pair_weight, aux_screen):
    det_local, rows, nocc = orbitals.shape
    capacity = pair_left.shape[0]
    n_det = lax.axis_size("det")
    n_orb = lax.axis_size("orb")
    me = lax.axis_index("det")
    slot_index = jnp.arange(capacity, dtype=jnp.int32)
    weights = jnp.where(slot_index < pair_count[0], pair_weight, jnp.zeros_like(pair_weight))
    left_local = pair_left % det_local
    left_rows = jnp.take(orbitals, left_local, axis=0)

    pad = 16
    marks = jnp.zeros((pad, nocc), jnp.bfloat16).at[0, :capacity].set(pair_right.astype(jnp.bfloat16))
    carried = jnp.concatenate([orbitals.reshape(det_local * rows, nocc), marks], axis=0)
    everyone = lax.all_gather(carried, "det", axis=0, tiled=False)
    right_all = everyone[:, det_local * rows, :capacity].astype(jnp.int32).reshape(-1)
    fetched = everyone[:, : det_local * rows].reshape(n_det * det_local, rows, nocc)
    left_full = gather_rows(left_rows, n_orb)
    right_rows = fetched[pair_right]
    right_full = gather_rows(right_rows, n_orb)

    left_stack = jnp.transpose(left_full, (1, 0, 2)).reshape(n_orb * rows, capacity * nocc)
    projected_t = jnp.einsum(
        "qst,tk->qsk", dfit, left_stack, preferred_element_type=jnp.float32
    ).astype(jnp.bfloat16).reshape(dfit.shape[0], n_orb * rows, capacity, nocc)

    correlation = jnp.einsum("brc,brd->bcd", left_full, right_full, preferred_element_type=jnp.float32)
    inverse = newton(correlation)
    moved_full = jnp.einsum(
        "brc,bcd->brd", right_full.astype(jnp.float32), inverse, precision=HI
    ).astype(jnp.bfloat16)
    moved_stack = jnp.transpose(moved_full, (1, 0, 2)).reshape(n_orb * rows, capacity * nocc)
    applied = jnp.einsum(
        "qst,tk->qsk", dfit, moved_stack, preferred_element_type=jnp.float32
    ).astype(jnp.bfloat16).reshape(dfit.shape[0], n_orb * rows, capacity, nocc)

    exchange = jnp.einsum("qtbc,btd->bqcd", projected_t, moved_full, preferred_element_type=jnp.float32)
    factor = 2.0 * weights[:, None, None, None] * aux_screen.astype(jnp.float32)[:, :, None, None]
    scaled = (factor * exchange).astype(jnp.bfloat16)
    moved_term = jnp.einsum("qsbc,bqcd->bsd", projected_t, scaled, preferred_element_type=jnp.float32)
    moved_grad = scatter_rows(moved_term, n_orb)
    live = (weights != 0.0)[:, None, None]
    right_grad = jnp.where(live, jnp.einsum("brc,bdc->brd", moved_grad, inverse, precision=HI), 0.0)

    came = lax.all_gather(right_grad, "det", axis=0, tiled=False)

    left_term = jnp.einsum("qsbc,bqdc->bsd", applied, scaled, preferred_element_type=jnp.float32)
    left_grad = jnp.where(live, scatter_rows(left_term, n_orb), 0.0)
    own = left_local[:, None] == jnp.arange(det_local, dtype=jnp.int32)[None, :]
    own_sum = jnp.sum(jnp.where(own[:, :, None, None], left_grad[:, None], 0.0), axis=0)

    asked = right_all.reshape(n_det, capacity)
    mine = asked[:, :, None] == (me * det_local + jnp.arange(det_local, dtype=jnp.int32))[None, None, :]
    returned = jnp.sum(jnp.where(mine[:, :, :, None, None], came[:, :, None], 0.0), axis=(0, 1))
    return own_sum + returned


def solution(mesh):
    in_specs = (
        P("det", "orb", None),
        P("orb", None, None),
        P("det"),
        P("det"),
        P("det"),
        P("det"),
        P("det", "orb"),
    )
    out_specs = P("det", "orb", None)
    return jax.shard_map(local_body, mesh=mesh, in_specs=in_specs, out_specs=out_specs, check_vma=False)
```

```python
import jax
import jax.numpy as jnp
from jax import lax
from jax.sharding import PartitionSpec as P

NS = 3
HI = lax.Precision.HIGHEST


def newton(correlation):
    eye = jnp.eye(correlation.shape[-1], dtype=jnp.float32)
    inverse = 2.0 * eye - correlation
    for _ in range(NS - 1):
        product = jnp.einsum("bij,bjk->bik", correlation, inverse, precision=HI)
        inverse = jnp.einsum("bij,bjk->bik", inverse, 2.0 * eye - product, precision=HI)
    return inverse


def gather_rows(rows_local, n_orb):
    spread = jnp.broadcast_to(rows_local[None], (n_orb,) + rows_local.shape)
    got = lax.all_to_all(spread, "orb", 0, 0, tiled=True)
    count, rows, nocc = rows_local.shape
    return jnp.transpose(got, (1, 0, 2, 3)).reshape(count, n_orb * rows, nocc)


def scatter_rows(parts):
    got = lax.all_to_all(parts, "orb", 0, 0, tiled=True)
    return jnp.sum(got, axis=0)


def local_body(orbitals, dfit, pair_left, pair_right, pair_count, pair_weight, aux_screen):
    det_local, rows, nocc = orbitals.shape
    capacity = pair_left.shape[0]
    n_det = lax.axis_size("det")
    n_orb = lax.axis_size("orb")
    me = lax.axis_index("det")
    slot_index = jnp.arange(capacity, dtype=jnp.int32)
    weights = jnp.where(slot_index < pair_count[0], pair_weight, jnp.zeros_like(pair_weight))
    left_local = pair_left % det_local
    left_rows = jnp.take(orbitals, left_local, axis=0)

    pad = 16
    marks = jnp.zeros((pad, nocc), jnp.bfloat16).at[0, :capacity].set(pair_right.astype(jnp.bfloat16))
    carried = jnp.concatenate([orbitals.reshape(det_local * rows, nocc), marks], axis=0)
    everyone = lax.all_gather(carried, "det", axis=0, tiled=False)
    right_all = everyone[:, det_local * rows, :capacity].astype(jnp.int32).reshape(-1)
    fetched = everyone[:, : det_local * rows].reshape(n_det * det_local, rows, nocc)
    left_full = gather_rows(left_rows, n_orb)
    right_rows = fetched[pair_right]
    right_full = gather_rows(right_rows, n_orb)

    left_stack = jnp.transpose(left_full, (1, 0, 2)).reshape(n_orb * rows, capacity * nocc)
    projected_t = jnp.einsum(
        "qst,tk->qsk", dfit, left_stack, preferred_element_type=jnp.float32
    ).astype(jnp.bfloat16).reshape(dfit.shape[0], n_orb * rows, capacity, nocc)

    correlation = jnp.einsum("brc,brd->bcd", left_full, right_full, preferred_element_type=jnp.float32)
    inverse = newton(correlation)
    moved_full = jnp.einsum(
        "brc,bcd->brd", right_full.astype(jnp.float32), inverse, precision=HI
    ).astype(jnp.bfloat16)
    moved_stack = jnp.transpose(moved_full, (1, 0, 2)).reshape(n_orb * rows, capacity * nocc)
    applied = jnp.einsum(
        "qst,tk->qsk", dfit, moved_stack, preferred_element_type=jnp.float32
    ).astype(jnp.bfloat16).reshape(dfit.shape[0], n_orb * rows, capacity, nocc)

    exchange = jnp.einsum("qtbc,btd->bqcd", projected_t, moved_full, preferred_element_type=jnp.float32)
    factor = 2.0 * weights[:, None, None, None] * aux_screen.astype(jnp.float32)[:, :, None, None]
    scaled = (factor * exchange).astype(jnp.bfloat16)
    blocks = (dfit.shape[0], n_orb, rows, capacity, nocc)
    moved_term = jnp.einsum(
        "qorbc,bqcd->obrd", projected_t.reshape(blocks), scaled, preferred_element_type=jnp.float32
    )
    moved_grad = scatter_rows(moved_term)
    live = (weights != 0.0)[:, None, None]
    right_grad = jnp.where(live, jnp.einsum("brc,bdc->brd", moved_grad, inverse, precision=HI), 0.0)

    came = lax.all_gather(right_grad, "det", axis=0, tiled=False)

    left_term = jnp.einsum(
        "qorbc,bqdc->obrd", applied.reshape(blocks), scaled, preferred_element_type=jnp.float32
    )
    left_grad = jnp.where(live, scatter_rows(left_term), 0.0)
    own = left_local[:, None] == jnp.arange(det_local, dtype=jnp.int32)[None, :]
    own_sum = jnp.sum(jnp.where(own[:, :, None, None], left_grad[:, None], 0.0), axis=0)

    asked = right_all.reshape(n_det, capacity)
    mine = asked[:, :, None] == (me * det_local + jnp.arange(det_local, dtype=jnp.int32))[None, None, :]
    returned = jnp.sum(jnp.where(mine[:, :, :, None, None], came[:, :, None], 0.0), axis=(0, 1))
    return own_sum + returned


def solution(mesh):
    in_specs = (
        P("det", "orb", None),
        P("orb", None, None),
        P("det"),
        P("det"),
        P("det"),
        P("det"),
        P("det", "orb"),
    )
    out_specs = P("det", "orb", None)
    return jax.shard_map(local_body, mesh=mesh, in_specs=in_specs, out_specs=out_specs, check_vma=False)
```

```python
import jax
import jax.numpy as jnp
from jax import lax
from jax.sharding import PartitionSpec as P

NS = 3
HI = lax.Precision.HIGHEST


def newton(correlation):
    eye = jnp.eye(correlation.shape[-1], dtype=jnp.float32)
    inverse = 2.0 * eye - correlation
    for _ in range(NS - 1):
        product = jnp.einsum("bij,bjk->bik", correlation, inverse, precision=HI)
        inverse = jnp.einsum("bij,bjk->bik", inverse, 2.0 * eye - product, precision=HI)
    return inverse


def gather_rows(rows_local, n_orb):
    spread = jnp.broadcast_to(rows_local[None], (n_orb,) + rows_local.shape)
    got = lax.all_to_all(spread, "orb", 0, 0, tiled=True)
    count, rows, nocc = rows_local.shape
    return jnp.transpose(got, (1, 0, 2, 3)).reshape(count, n_orb * rows, nocc)


def row_blocks(full, n_orb):
    count, total, nocc = full.shape
    return jnp.transpose(full.reshape(count, n_orb, total // n_orb, nocc), (1, 0, 2, 3))


def scatter_rows(full, n_orb, parts=None):
    parts = row_blocks(full, n_orb) if parts is None else parts
    got = lax.all_to_all(parts, "orb", 0, 0, tiled=True)
    return jnp.sum(got, axis=0)


def local_body(orbitals, dfit, pair_left, pair_right, pair_count, pair_weight, aux_screen):
    det_local, rows, nocc = orbitals.shape
    capacity = pair_left.shape[0]
    n_det = lax.axis_size("det")
    n_orb = lax.axis_size("orb")
    me = lax.axis_index("det")
    slot_index = jnp.arange(capacity, dtype=jnp.int32)
    weights = jnp.where(slot_index < pair_count[0], pair_weight, jnp.zeros_like(pair_weight))
    left_local = pair_left % det_local
    left_rows = jnp.take(orbitals, left_local, axis=0)

    pad = 16
    marks = jnp.zeros((pad, nocc), jnp.bfloat16).at[0, :capacity].set(pair_right.astype(jnp.bfloat16))
    carried = jnp.concatenate([orbitals.reshape(det_local * rows, nocc), marks], axis=0)
    everyone = lax.all_gather(carried, "det", axis=0, tiled=False)
    right_all = everyone[:, det_local * rows, :capacity].astype(jnp.int32).reshape(-1)
    fetched = everyone[:, : det_local * rows].reshape(n_det * det_local, rows, nocc)
    left_full = gather_rows(left_rows, n_orb)
    right_rows = fetched[pair_right]
    right_full = gather_rows(right_rows, n_orb)

    left_stack = jnp.transpose(left_full, (1, 0, 2)).reshape(n_orb * rows, capacity * nocc)
    projected_t = jnp.einsum(
        "qst,tk->qsk", dfit, left_stack, preferred_element_type=jnp.float32
    ).astype(jnp.bfloat16).reshape(dfit.shape[0], n_orb * rows, capacity, nocc)

    correlation = jnp.einsum("brc,brd->bcd", left_full, right_full, preferred_element_type=jnp.float32)
    inverse = newton(correlation)
    moved_full = jnp.einsum(
        "brc,bcd->brd", right_full.astype(jnp.float32), inverse, precision=HI
    ).astype(jnp.bfloat16)
    moved_stack = jnp.transpose(moved_full, (1, 0, 2)).reshape(n_orb * rows, capacity * nocc)
    applied = jnp.einsum(
        "qst,tk->qsk", dfit, moved_stack, preferred_element_type=jnp.float32
    ).astype(jnp.bfloat16).reshape(dfit.shape[0], n_orb * rows, capacity, nocc)

    exchange = jnp.einsum("qtbc,btd->bqcd", projected_t, moved_full, preferred_element_type=jnp.float32)
    factor = 2.0 * weights[:, None, None, None] * aux_screen.astype(jnp.float32)[:, :, None, None]
    scaled = (factor * exchange).astype(jnp.bfloat16)
    moved_term = jnp.einsum("qsbc,bqcd->bsd", projected_t, scaled, preferred_element_type=jnp.float32)
    moved_grad = scatter_rows(moved_term, n_orb)
    live = (weights != 0.0)[:, None, None]
    right_grad = jnp.where(live, jnp.einsum("brc,bdc->brd", moved_grad, inverse, precision=HI), 0.0)

    came = lax.all_gather(right_grad, "det", axis=0, tiled=False)

    left_term = jnp.einsum("qsbc,bqdc->bsd", applied, scaled, preferred_element_type=jnp.float32)
    left_parts = row_blocks(left_term, n_orb)
    left_grad = jnp.where(live, scatter_rows(None, n_orb, left_parts), 0.0)
    own = left_local[:, None] == jnp.arange(det_local, dtype=jnp.int32)[None, :]
    own_sum = jnp.sum(jnp.where(own[:, :, None, None], left_grad[:, None], 0.0), axis=0)

    asked = right_all.reshape(n_det, capacity)
    mine = asked[:, :, None] == (me * det_local + jnp.arange(det_local, dtype=jnp.int32))[None, None, :]
    returned = jnp.sum(jnp.where(mine[:, :, :, None, None], came[:, :, None], 0.0), axis=(0, 1))
    return own_sum + returned


def solution(mesh):
    in_specs = (
        P("det", "orb", None),
        P("orb", None, None),
        P("det"),
        P("det"),
        P("det"),
        P("det"),
        P("det", "orb"),
    )
    out_specs = P("det", "orb", None)
    return jax.shard_map(local_body, mesh=mesh, in_specs=in_specs, out_specs=out_specs, check_vma=False)
```

```python
import jax
import jax.numpy as jnp
from jax import lax
from jax.sharding import PartitionSpec as P

NS = 3
HI = lax.Precision.HIGHEST


def newton(correlation):
    eye = jnp.eye(correlation.shape[-1], dtype=jnp.float32)
    inverse = 2.0 * eye - correlation
    for _ in range(NS - 1):
        product = jnp.einsum("bij,bjk->bik", correlation, inverse, precision=HI)
        inverse = jnp.einsum("bij,bjk->bik", inverse, 2.0 * eye - product, precision=HI)
    return inverse


def gather_rows(rows_local, n_orb):
    spread = jnp.broadcast_to(rows_local[None], (n_orb,) + rows_local.shape)
    got = lax.all_to_all(spread, "orb", 0, 0, tiled=True)
    count, rows, nocc = rows_local.shape
    return jnp.transpose(got, (1, 0, 2, 3)).reshape(count, n_orb * rows, nocc)


def row_blocks(full, n_orb):
    count, total, nocc = full.shape
    return jnp.transpose(full.reshape(count, n_orb, total // n_orb, nocc), (1, 0, 2, 3))


def scatter_rows(full, n_orb, parts=None):
    parts = row_blocks(full, n_orb) if parts is None else parts
    got = lax.all_to_all(parts, "orb", 0, 0, tiled=True)
    return jnp.sum(got, axis=0)


def local_body(orbitals, dfit, pair_left, pair_right, pair_count, pair_weight, aux_screen):
    det_local, rows, nocc = orbitals.shape
    capacity = pair_left.shape[0]
    n_det = lax.axis_size("det")
    n_orb = lax.axis_size("orb")
    me = lax.axis_index("det")
    slot_index = jnp.arange(capacity, dtype=jnp.int32)
    weights = jnp.where(slot_index < pair_count[0], pair_weight, jnp.zeros_like(pair_weight))
    left_local = pair_left % det_local
    left_rows = jnp.take(orbitals, left_local, axis=0)

    pad = 16
    marks = jnp.zeros((pad, nocc), jnp.bfloat16).at[0, :capacity].set(pair_right.astype(jnp.bfloat16))
    carried = jnp.concatenate([orbitals.reshape(det_local * rows, nocc), marks], axis=0)
    everyone = lax.all_gather(carried, "det", axis=0, tiled=False)
    right_all = everyone[:, det_local * rows, :capacity].astype(jnp.int32).reshape(-1)
    left_full = gather_rows(left_rows, n_orb)
    right_rows = jnp.stack([
        lax.dynamic_slice(everyone, (pair_right[k] // det_local, (pair_right[k] % det_local) * rows, 0), (1, rows, nocc))[0]
        for k in range(capacity)
    ])
    right_full = gather_rows(right_rows, n_orb)

    left_stack = jnp.transpose(left_full, (1, 0, 2)).reshape(n_orb * rows, capacity * nocc)
    projected_t = jnp.einsum(
        "qst,tk->qsk", dfit, left_stack, preferred_element_type=jnp.float32
    ).astype(jnp.bfloat16).reshape(dfit.shape[0], n_orb * rows, capacity, nocc)

    correlation = jnp.einsum("brc,brd->bcd", left_full, right_full, preferred_element_type=jnp.float32)
    inverse = newton(correlation)
    moved_full = jnp.einsum(
        "brc,bcd->brd", right_full.astype(jnp.float32), inverse, precision=HI
    ).astype(jnp.bfloat16)
    moved_stack = jnp.transpose(moved_full, (1, 0, 2)).reshape(n_orb * rows, capacity * nocc)
    applied = jnp.einsum(
        "qst,tk->qsk", dfit, moved_stack, preferred_element_type=jnp.float32
    ).astype(jnp.bfloat16).reshape(dfit.shape[0], n_orb * rows, capacity, nocc)

    exchange = jnp.einsum("qtbc,btd->bqcd", projected_t, moved_full, preferred_element_type=jnp.float32)
    factor = 2.0 * weights[:, None, None, None] * aux_screen.astype(jnp.float32)[:, :, None, None]
    scaled = (factor * exchange).astype(jnp.bfloat16)
    moved_term = jnp.einsum("qsbc,bqcd->bsd", projected_t, scaled, preferred_element_type=jnp.float32)
    moved_grad = scatter_rows(moved_term, n_orb)
    live = (weights != 0.0)[:, None, None]
    right_grad = jnp.where(live, jnp.einsum("brc,bdc->brd", moved_grad, inverse, precision=HI), 0.0)

    came = lax.all_gather(right_grad, "det", axis=0, tiled=False)

    left_term = jnp.einsum("qsbc,bqdc->bsd", applied, scaled, preferred_element_type=jnp.float32)
    left_parts = row_blocks(left_term, n_orb)
    left_grad = jnp.where(live, scatter_rows(None, n_orb, left_parts), 0.0)
    own = left_local[:, None] == jnp.arange(det_local, dtype=jnp.int32)[None, :]
    own_sum = jnp.sum(jnp.where(own[:, :, None, None], left_grad[:, None], 0.0), axis=0)

    asked = right_all.reshape(n_det, capacity)
    mine = asked[:, :, None] == (me * det_local + jnp.arange(det_local, dtype=jnp.int32))[None, None, :]
    returned = jnp.sum(jnp.where(mine[:, :, :, None, None], came[:, :, None], 0.0), axis=(0, 1))
    return own_sum + returned


def solution(mesh):
    in_specs = (
        P("det", "orb", None),
        P("orb", None, None),
        P("det"),
        P("det"),
        P("det"),
        P("det"),
        P("det", "orb"),
    )
    out_specs = P("det", "orb", None)
    return jax.shard_map(local_body, mesh=mesh, in_specs=in_specs, out_specs=out_specs, check_vma=False)
```

```python
import jax
import jax.numpy as jnp
from jax import lax
from jax.sharding import PartitionSpec as P

NS = 3
HI = lax.Precision.HIGHEST


def newton(correlation):
    eye = jnp.eye(correlation.shape[-1], dtype=jnp.float32)
    inverse = 2.0 * eye - correlation
    for _ in range(NS - 1):
        product = jnp.einsum("bij,bjk->bik", correlation, inverse, precision=HI)
        inverse = jnp.einsum("bij,bjk->bik", inverse, 2.0 * eye - product, precision=HI)
    return inverse


def gather_rows(rows_local, n_orb):
    spread = jnp.broadcast_to(rows_local[None], (n_orb,) + rows_local.shape)
    got = lax.all_to_all(spread, "orb", 0, 0, tiled=True)
    count, rows, nocc = rows_local.shape
    return jnp.transpose(got, (1, 0, 2, 3)).reshape(count, n_orb * rows, nocc)


def row_blocks(full, n_orb):
    count, total, nocc = full.shape
    return jnp.transpose(full.reshape(count, n_orb, total // n_orb, nocc), (1, 0, 2, 3))


def scatter_rows(full, n_orb, parts=None):
    parts = row_blocks(full, n_orb) if parts is None else parts
    got = lax.all_to_all(parts, "orb", 0, 0, tiled=True)
    return jnp.sum(got, axis=0)


def local_body(orbitals, dfit, pair_left, pair_right, pair_count, pair_weight, aux_screen):
    det_local, rows, nocc = orbitals.shape
    capacity = pair_left.shape[0]
    n_det = lax.axis_size("det")
    n_orb = lax.axis_size("orb")
    me = lax.axis_index("det")
    slot_index = jnp.arange(capacity, dtype=jnp.int32)
    weights = jnp.where(slot_index < pair_count[0], pair_weight, jnp.zeros_like(pair_weight))
    left_local = pair_left % det_local
    left_rows = jnp.take(orbitals, left_local, axis=0)

    everyone = lax.all_gather(orbitals.reshape(det_local * rows, nocc), "det", axis=0, tiled=False)
    right_all = lax.all_to_all(
        jnp.broadcast_to(pair_right[None], (n_det, capacity)), "det", 0, 0, tiled=True
    ).reshape(n_det * capacity)
    left_full = gather_rows(left_rows, n_orb)
    early = jnp.minimum(jnp.min(right_all), 0)
    right_rows = jnp.stack([
        lax.dynamic_slice(
            everyone, (pair_right[k] // det_local + early, (pair_right[k] % det_local) * rows, 0), (1, rows, nocc)
        )[0]
        for k in range(capacity)
    ])
    right_full = gather_rows(right_rows, n_orb)

    left_stack = jnp.transpose(left_full, (1, 0, 2)).reshape(n_orb * rows, capacity * nocc)
    projected_t = jnp.einsum(
        "qst,tk->qsk", dfit, left_stack, preferred_element_type=jnp.float32
    ).astype(jnp.bfloat16).reshape(dfit.shape[0], n_orb * rows, capacity, nocc)

    correlation = jnp.einsum("brc,brd->bcd", left_full, right_full, preferred_element_type=jnp.float32)
    inverse = newton(correlation)
    moved_full = jnp.einsum(
        "brc,bcd->brd", right_full.astype(jnp.float32), inverse, precision=HI
    ).astype(jnp.bfloat16)
    moved_stack = jnp.transpose(moved_full, (1, 0, 2)).reshape(n_orb * rows, capacity * nocc)
    applied = jnp.einsum(
        "qst,tk->qsk", dfit, moved_stack, preferred_element_type=jnp.float32
    ).astype(jnp.bfloat16).reshape(dfit.shape[0], n_orb * rows, capacity, nocc)

    exchange = jnp.einsum("qtbc,btd->bqcd", projected_t, moved_full, preferred_element_type=jnp.float32)
    factor = 2.0 * weights[:, None, None, None] * aux_screen.astype(jnp.float32)[:, :, None, None]
    scaled = (factor * exchange).astype(jnp.bfloat16)
    moved_term = jnp.einsum("qsbc,bqcd->bsd", projected_t, scaled, preferred_element_type=jnp.float32)
    moved_grad = scatter_rows(moved_term, n_orb)
    live = (weights != 0.0)[:, None, None]
    right_grad = jnp.where(live, jnp.einsum("brc,bdc->brd", moved_grad, inverse, precision=HI), 0.0)

    came = lax.all_gather(right_grad, "det", axis=0, tiled=False)

    left_term = jnp.einsum("qsbc,bqdc->bsd", applied, scaled, preferred_element_type=jnp.float32)
    left_parts = row_blocks(left_term, n_orb)
    left_grad = jnp.where(live, scatter_rows(None, n_orb, left_parts), 0.0)
    own = left_local[:, None] == jnp.arange(det_local, dtype=jnp.int32)[None, :]
    own_sum = jnp.sum(jnp.where(own[:, :, None, None], left_grad[:, None], 0.0), axis=0)

    asked = right_all.reshape(n_det, capacity)
    mine = asked[:, :, None] == (me * det_local + jnp.arange(det_local, dtype=jnp.int32))[None, None, :]
    returned = jnp.sum(jnp.where(mine[:, :, :, None, None], came[:, :, None], 0.0), axis=(0, 1))
    return own_sum + returned


def solution(mesh):
    in_specs = (
        P("det", "orb", None),
        P("orb", None, None),
        P("det"),
        P("det"),
        P("det"),
        P("det"),
        P("det", "orb"),
    )
    out_specs = P("det", "orb", None)
    return jax.shard_map(local_body, mesh=mesh, in_specs=in_specs, out_specs=out_specs, check_vma=False)
```

```python
import jax
import jax.numpy as jnp
from jax import lax
from jax.sharding import PartitionSpec as P

NS = 3
HI = lax.Precision.HIGHEST


def newton(correlation):
    eye = jnp.eye(correlation.shape[-1], dtype=jnp.float32)
    inverse = 2.0 * eye - correlation
    for _ in range(NS - 1):
        product = jnp.einsum("bij,bjk->bik", correlation, inverse, precision=HI)
        inverse = jnp.einsum("bij,bjk->bik", inverse, 2.0 * eye - product, precision=HI)
    return inverse


def gather_rows(rows_local, n_orb):
    spread = jnp.broadcast_to(rows_local[None], (n_orb,) + rows_local.shape)
    got = lax.all_to_all(spread, "orb", 0, 0, tiled=True)
    count, rows, nocc = rows_local.shape
    return jnp.transpose(got, (1, 0, 2, 3)).reshape(count, n_orb * rows, nocc)


def row_blocks(full, n_orb):
    count, total, nocc = full.shape
    return jnp.transpose(full.reshape(count, n_orb, total // n_orb, nocc), (1, 0, 2, 3))


def scatter_rows(full, n_orb, parts=None):
    parts = row_blocks(full, n_orb) if parts is None else parts
    got = lax.all_to_all(parts, "orb", 0, 0, tiled=True)
    return jnp.sum(got, axis=0)


def local_body(orbitals, dfit, pair_left, pair_right, pair_count, pair_weight, aux_screen):
    det_local, rows, nocc = orbitals.shape
    capacity = pair_left.shape[0]
    n_det = lax.axis_size("det")
    n_orb = lax.axis_size("orb")
    me = lax.axis_index("det")
    slot_index = jnp.arange(capacity, dtype=jnp.int32)
    weights = jnp.where(slot_index < pair_count[0], pair_weight, jnp.zeros_like(pair_weight))
    left_local = pair_left % det_local
    left_rows = jnp.take(orbitals, left_local, axis=0)

    pad = 16
    marks = jnp.zeros((pad, nocc), jnp.bfloat16).at[0, :capacity].set(pair_right.astype(jnp.bfloat16))
    carried = jnp.concatenate([orbitals.reshape(det_local * rows, nocc), marks], axis=0)
    everyone = lax.all_gather(carried, "det", axis=0, tiled=False)
    right_all = everyone[:, det_local * rows, :capacity].astype(jnp.int32).reshape(-1)
    left_full = gather_rows(left_rows, n_orb)
    right_rows = jnp.stack([
        lax.dynamic_slice(everyone, (pair_right[k] // det_local, (pair_right[k] % det_local) * rows, 0), (1, rows, nocc))[0]
        for k in range(capacity)
    ])
    right_full = gather_rows(right_rows, n_orb)

    left_stack = jnp.transpose(left_full, (1, 0, 2)).reshape(n_orb * rows, capacity * nocc)
    projected_t = jnp.einsum(
        "qst,tk->qsk", dfit, left_stack, preferred_element_type=jnp.float32
    ).astype(jnp.bfloat16).reshape(dfit.shape[0], n_orb * rows, capacity, nocc)

    correlation = jnp.einsum("brc,brd->bcd", left_full, right_full, preferred_element_type=jnp.float32)
    inverse = newton(correlation)
    moved_full = jnp.einsum(
        "brc,bcd->brd", right_full.astype(jnp.float32), inverse, precision=HI
    ).astype(jnp.bfloat16)
    moved_stack = jnp.transpose(moved_full, (1, 0, 2)).reshape(n_orb * rows, capacity * nocc)
    applied = jnp.einsum(
        "qst,tk->qsk", dfit, moved_stack, preferred_element_type=jnp.float32
    ).astype(jnp.bfloat16).reshape(dfit.shape[0], n_orb * rows, capacity, nocc)

    exchange = jnp.einsum("qtbc,btd->bqcd", projected_t, moved_full, preferred_element_type=jnp.float32)
    factor = 2.0 * weights[:, None, None, None] * aux_screen.astype(jnp.float32)[:, :, None, None]
    scaled = (factor * exchange).astype(jnp.bfloat16)
    moved_term = jnp.einsum("qsbc,bqcd->bsd", projected_t, scaled, preferred_element_type=jnp.float32)
    moved_grad = scatter_rows(moved_term, n_orb)
    live = (weights != 0.0)[:, None, None]
    right_grad = jnp.where(live, jnp.einsum("brc,bdc->brd", moved_grad, inverse, precision=HI), 0.0)

    came = lax.all_gather(right_grad, "det", axis=0, tiled=False)

    left_term = jnp.einsum("qsbc,bqdc->bsd", applied, scaled, preferred_element_type=jnp.float32)
    left_parts = row_blocks(left_term, n_orb)
    left_grad = jnp.where(live, scatter_rows(None, n_orb, left_parts), 0.0)
    own = left_local[:, None] == jnp.arange(det_local, dtype=jnp.int32)[None, :]
    own_sum = jnp.sum(jnp.where(own[:, :, None, None], left_grad[:, None], 0.0), axis=0)

    target = jnp.where(right_all // det_local == me, right_all % det_local, det_local)
    returned = jnp.zeros((det_local, rows, nocc), jnp.float32).at[target].add(
        came.reshape(n_det * capacity, rows, nocc), mode="drop"
    )
    return own_sum + returned


def solution(mesh):
    in_specs = (
        P("det", "orb", None),
        P("orb", None, None),
        P("det"),
        P("det"),
        P("det"),
        P("det"),
        P("det", "orb"),
    )
    out_specs = P("det", "orb", None)
    return jax.shard_map(local_body, mesh=mesh, in_specs=in_specs, out_specs=out_specs, check_vma=False)
```
